512 devices in a mesh: harm: 8 (over x, z_hi), space: 64 (over z_lo, y, core).
Axes of the slice: x: 4, y: 4, z: 16 (z_hi: 2, z_lo: 8; z = z_hi * 8 + z_lo), core: 2. Of those that a mesh axis runs over, the one named last changes fastest.
Arguments:
- rhs_field: float32 [64, 16384], P('harm', 'space'), may hold values from -14 to 14
- neighbors: int32 [8, 16384], P(None, 'space'), may hold values from 0 to 16383, as said below
- nu_mean: float32 [8, 16384], P(None, 'space'), may hold values from 0.5 to 4
- nu_ripple: float32 [64, 8, 16384], P(None, None, 'space'), may hold values from -0.24 to 0.24
- mass_coeff: float32 [16384], P('space'), may hold values from 0.5 to 2
- eddy_coeff: float32 [16384], P('space'), may hold values from 0.25 to 2
Outputs:
- correction: float32 [64, 16384], P('harm', 'space')
- residual: float32 [64, 16384], P('harm', 'space')
The draws below stay inside these ranges and needn't reach their ends.
Inputs may be any that keep to these rules, and one draw needn't show every extreme that they name: neighbors[d, n] is a node at most 64 places from n in the node order closed into a loop (node 16383 lies next to node 0), or n itself for an unused slot; slot 0 is always used, and some entry lies 64 places away in each direction.
All inputs are finite; a program needn't handle non-finite values.
Results may differ from the reference program's by a relative error of at most 0.0003.
Values sent between devices are 32-bit elements; how exact they have to be, the bound alone decides.
No kernel may reach another device: no remote copies, remote signals or barrier semaphores. Data moves between devices by JAX's collectives and lax.ppermute only.
A program may use at most 64 MiB of HBM per device.

```python
import math
import jax
import jax.numpy as jnp
from jax import lax

H = 64
DEG = 8
IF = 64
ITERS = 8
NODES = 16384


def draw_rhs_field(key, part):
    k_noise, k_rows, k_cols = jax.random.split(key, 3)
    position = jnp.arange(NODES, dtype=jnp.float32)
    column_scale = jnp.exp(jnp.log(3.0) * position / max(NODES - 1, 1) + jax.random.uniform(k_cols, (NODES,), minval=0.0, maxval=jnp.log(3.0)))
    noise = jnp.clip(jax.random.normal(k_noise, (H, NODES)), -4.0, 4.0)
    row_scale = jnp.exp(jax.random.uniform(k_rows, (H, 1), minval=jnp.log(0.25), maxval=0.0))
    return (noise * row_scale * column_scale[None, :] / 3.0).astype(jnp.float32)


def draw_neighbors(key, part):
    k_step, k_live = jax.random.split(key)
    position = jnp.arange(NODES, dtype=jnp.int32)
    stride = jax.random.randint(k_step, (DEG, NODES), -IF, IF + 1)
    live_slots = jax.random.randint(k_live, (1, NODES), 2, DEG + 1)
    slot_index = jnp.arange(DEG, dtype=jnp.int32)[:, None]
    stride = jnp.where(slot_index < live_slots, stride, 0)
    stride = stride.at[0, 0].set(IF).at[0, 1].set(-IF)
    return jnp.mod(position[None, :] + stride, NODES).astype(jnp.int32)


def levels(stream_key, shape, cuts, low, high):
    factor_of, own = 1.0, jax.random.fold_in(stream_key, 6)
    for dim, parts in cuts:
        steps = jnp.exp(jax.random.uniform(jax.random.fold_in(own, dim), (parts,), jnp.float32, low / len(cuts), high / len(cuts)))
        factor_of = factor_of * jnp.repeat(steps, shape[dim] // parts).reshape([-1 if axis == dim else 1 for axis in range(len(shape))])
    return factor_of


def gaussian(key, extent, spread, limit, cuts=(), kind=jnp.bfloat16):
    result = jax.random.normal(key, extent, jnp.float32) * spread
    if len(cuts) > 0:
        result = levels(key, extent, cuts, -0.22, 0.18) * result
    return jnp.clip(result, min=-limit, max=limit).astype(kind)


def setup_inputs(seed: int = 0) -> dict:
    arg_keys = jax.random.split(jax.random.key(seed), 7)
    rhs_field = draw_rhs_field(jax.random.fold_in(arg_keys[6], 71), 0)
    neighbors = draw_neighbors(jax.random.fold_in(arg_keys[6], 71), 0)
    nu_mean = jnp.clip(jnp.exp(math.log(4.0) - 2.0794415 * jax.random.uniform(arg_keys[2], (DEG, NODES), jnp.float32) ** levels(arg_keys[2], (DEG, NODES), ((1, 64),), -0.2, 0.2)), 0.5, 4.0)
    nu_ripple = gaussian(arg_keys[3], (H, DEG, NODES), 0.04, 0.24, ((2, 64),), jnp.float32)
    mass_coeff = jnp.clip(jnp.exp(math.log(2.0) - 1.3862944 * jax.random.uniform(arg_keys[4], (NODES,), jnp.float32) ** levels(arg_keys[4], (NODES,), ((0, 64),), -0.2, 0.2)), 0.5, 2.0)
    eddy_coeff = jnp.clip(jnp.exp(math.log(2.0) - 2.0794415 * jax.random.uniform(arg_keys[5], (NODES,), jnp.float32) ** levels(arg_keys[5], (NODES,), ((0, 64),), -0.2, 0.2)), 0.25, 2.0)
    return {"rhs_field": rhs_field, "neighbors": neighbors, "nu_mean": nu_mean, "nu_ripple": nu_ripple, "mass_coeff": mass_coeff, "eddy_coeff": eddy_coeff}


def eddy_factor(harmonics):
    harm_order = (jnp.arange(harmonics) // 2 + 1).astype(jnp.float32)
    sign_vals = jnp.where(jnp.arange(harmonics) % 2 == 0, 1.0, -1.0).astype(jnp.float32)
    return 4.0 * harm_order / harmonics * sign_vals

def swap_pairs(vector_in):
    shaped = vector_in.reshape(vector_in.shape[0] // 2, 2, vector_in.shape[1])
    return shaped[:, ::-1, :].reshape(vector_in.shape)

def apply_operator(vector_in, kernel_hat, neighbors, mass_coeff, eddy_coeff, factor):
    gradients = vector_in[:, None, :] - vector_in[:, neighbors]
    fluxes = jnp.fft.irfft(kernel_hat * jnp.fft.rfft(gradients, axis=0), n=vector_in.shape[0], axis=0)
    fluxes = fluxes.astype(jnp.float32)
    return lax.optimization_barrier(jnp.sum(fluxes, axis=1)) + mass_coeff[None, :] * vector_in + eddy_coeff[None, :] * factor[:, None] * swap_pairs(vector_in)

def least_squares(columns, beta_norm):
    steps_total = len(columns)
    rot_cos, rot_sin = ([], [])
    target = [beta_norm] + [jnp.zeros((), jnp.float32)] * steps_total
    triangle = []
    for j in range(steps_total):
        column_vals = list(columns[j])
        for i in range(j):
            first, second = (column_vals[i], column_vals[i + 1])
            column_vals[i] = rot_cos[i] * first + rot_sin[i] * second
            column_vals[i + 1] = rot_cos[i] * second - rot_sin[i] * first
        radius = jnp.sqrt(column_vals[j] * column_vals[j] + column_vals[j + 1] * column_vals[j + 1])
        cosine = column_vals[j] / radius
        sine_val = column_vals[j + 1] / radius
        rot_cos.append(cosine)
        rot_sin.append(sine_val)
        column_vals[j] = radius
        target[j + 1] = -sine_val * target[j]
        target[j] = cosine * target[j]
        triangle.append(column_vals[:j + 1])
    coeffs = [None] * steps_total
    for j in reversed(range(steps_total)):
        running = target[j]
        for k in range(j + 1, steps_total):
            running = running - triangle[k][j] * coeffs[k]
        coeffs[j] = running / triangle[j][j]
    return coeffs

def reference(rhs_field, neighbors, nu_mean, nu_ripple, mass_coeff, eddy_coeff):
    harmonics = rhs_field.shape[0]
    kernel = nu_ripple.at[0].add(nu_mean)
    kernel_hat = jnp.fft.rfft(kernel, axis=0)
    factor = eddy_factor(harmonics)

    def operate(vector_in):
        return apply_operator(vector_in, kernel_hat, neighbors, mass_coeff, eddy_coeff, factor)
    beta_norm = jnp.sqrt(jnp.sum(rhs_field * rhs_field))
    krylov = [rhs_field / beta_norm]
    columns = []
    for j in range(ITERS):
        image = operate(krylov[j])
        projected = [jnp.sum(krylov[i] * image) for i in range(j + 1)]
        for i in range(j + 1):
            image = image - projected[i] * krylov[i]
        length = jnp.sqrt(jnp.sum(image * image))
        columns.append(projected + [length])
        if j + 1 < ITERS:
            krylov.append(image / length)
    coeffs = least_squares(columns, beta_norm)
    correction = coeffs[0] * krylov[0]
    for j in range(1, ITERS):
        correction = correction + coeffs[j] * krylov[j]
    residual = rhs_field - operate(correction)
    return (correction, residual)
```

```python
import jax
import jax.numpy as jnp
from jax import lax
from jax.sharding import PartitionSpec as P

IF = 64
ITERS = 8


def with_halo(array, sides, width):
    for axis, dim in sides:
        count, length = (lax.axis_size(axis), array.shape[dim])
        up = [(i, (i + 1) % count) for i in range(count)]
        down = [(j, i) for i, j in up]
        last = lax.slice_in_dim(array, length - width, length, axis=dim)
        leading = lax.slice_in_dim(array, 0, width, axis=dim)
        before = lax.ppermute(last, axis, up)
        after = lax.ppermute(leading, axis, down)
        array = jnp.concatenate([before, array, after], axis=dim)
    return array


def swap_pairs(vector_in):
    shaped = vector_in.reshape(vector_in.shape[0] // 2, 2, vector_in.shape[1])
    return shaped[:, ::-1, :].reshape(vector_in.shape)


def fourier_tables(harmonics):
    index_vals = jnp.arange(harmonics, dtype=jnp.int32)
    product_mod = jnp.mod(index_vals[:, None] * index_vals[None, :], harmonics).astype(jnp.float32)
    phase = 2.0 * jnp.pi * product_mod / harmonics
    return (jnp.cos(phase), jnp.sin(phase))


def matmul_high(left, right):
    return jnp.dot(left, right, precision=lax.Precision.HIGHEST, preferred_element_type=jnp.float32)


def least_squares(columns, beta_norm):
    steps_total = len(columns)
    rot_cos, rot_sin = ([], [])
    target = [beta_norm] + [jnp.zeros((), jnp.float32)] * steps_total
    triangle = []
    for j in range(steps_total):
        column_vals = list(columns[j])
        for i in range(j):
            first, second = (column_vals[i], column_vals[i + 1])
            column_vals[i] = rot_cos[i] * first + rot_sin[i] * second
            column_vals[i + 1] = rot_cos[i] * second - rot_sin[i] * first
        radius = jnp.sqrt(column_vals[j] * column_vals[j] + column_vals[j + 1] * column_vals[j + 1])
        cosine = column_vals[j] / radius
        sine_val = column_vals[j + 1] / radius
        rot_cos.append(cosine)
        rot_sin.append(sine_val)
        column_vals[j] = radius
        target[j + 1] = -sine_val * target[j]
        target[j] = cosine * target[j]
        triangle.append(column_vals[: j + 1])
    coeffs = [None] * steps_total
    for j in reversed(range(steps_total)):
        running = target[j]
        for k in range(j + 1, steps_total):
            running = running - triangle[k][j] * coeffs[k]
        coeffs[j] = running / triangle[j][j]
    return coeffs


def all_sum(values):
    for axis in ("harm", "space"):
        count = lax.axis_size(axis)
        if count & (count - 1):
            values = lax.psum(values, axis)
            continue
        stride = 1
        while stride < count:
            values = values + lax.ppermute(values, axis, [(i, i ^ stride) for i in range(count)])
            stride *= 2
    return values


def per_device(rhs_field, neighbors, nu_mean, nu_ripple, mass_coeff, eddy_coeff):
    block, nodes_own = rhs_field.shape
    harmonics = nu_ripple.shape[0]
    halo_width = IF
    harm_start = lax.axis_index("harm") * block
    kernel = nu_ripple.at[0].add(nu_mean)
    cos_table, sin_table = fourier_tables(harmonics)
    total_nodes = nodes_own * lax.axis_size("space")
    relative = jnp.mod(neighbors - lax.axis_index("space") * nodes_own, total_nodes)
    relative = jnp.where(relative >= total_nodes - halo_width, relative - total_nodes, relative)
    ext_index = relative + halo_width
    global_harm = harm_start + jnp.arange(block)
    harm_order = (global_harm // 2 + 1).astype(jnp.float32)
    sign_vals = jnp.where(global_harm % 2 == 0, 1.0, -1.0).astype(jnp.float32)
    factor = 4.0 * harm_order / harmonics * sign_vals
    node_share = nodes_own // lax.axis_size("harm")
    kernel_use = lax.dynamic_slice_in_dim(
        kernel, lax.axis_index("harm") * node_share, node_share, 2
    )
    kernel_flat = kernel_use.reshape(harmonics, -1)
    kernel_real = matmul_high(cos_table, kernel_flat)
    kernel_imag = -matmul_high(sin_table, kernel_flat)

    def convolve_spectrum(spec_real, spec_imag, out_cos, out_sin):
        prod_real = spec_real * kernel_real - spec_imag * kernel_imag
        prod_imag = spec_real * kernel_imag + spec_imag * kernel_real
        return (matmul_high(out_cos, prod_real) - matmul_high(out_sin, prod_imag)) / harmonics

    def operate(vector_in):
        extended = with_halo(vector_in, (("space", 1),), halo_width)
        gradients = extended[:, None, halo_width : halo_width + nodes_own] - extended[:, ext_index]
        spread = lax.all_to_all(gradients, "harm", split_axis=2, concat_axis=0, tiled=True)
        spread_flat = spread.reshape(harmonics, -1)
        spec_real = matmul_high(cos_table, spread_flat)
        spec_imag = -matmul_high(sin_table, spread_flat)
        fluxes = convolve_spectrum(spec_real, spec_imag, cos_table, sin_table)
        fluxes = fluxes.reshape(spread.shape)
        fluxes = lax.all_to_all(fluxes, "harm", split_axis=0, concat_axis=2, tiled=True)
        return (
            jnp.sum(fluxes, axis=1)
            + mass_coeff[None, :] * vector_in
            + eddy_coeff[None, :] * factor[:, None] * swap_pairs(vector_in)
        )

    local_rows = lambda rows, other: jnp.sum(jnp.stack(rows) * other[None], axis=(1, 2))
    sums = all_sum(jnp.concatenate([local_rows([rhs_field], rhs_field), local_rows([rhs_field], image := operate(rhs_field))]))
    beta_norm = jnp.sqrt(sums[0])
    krylov = [rhs_field / beta_norm]
    images = [image / beta_norm]
    columns = [[sums[1] / beta_norm / beta_norm]]
    ortho = images[0] - columns[0][0] * krylov[0]
    for j in range(1, ITERS):
        image = operate(ortho)
        sums = all_sum(
            jnp.concatenate([local_rows([ortho], ortho), local_rows(krylov + [ortho], image)])
        )
        length = jnp.sqrt(sums[0])
        columns[j - 1].append(length)
        krylov.append(ortho / length)
        images.append(image / length)
        projected = [sums[1 + i] / length for i in range(j)] + [sums[1 + j] / length / length]
        columns.append(projected)
        ortho = images[j]
        for i in range(j + 1):
            ortho = ortho - projected[i] * krylov[i]
    columns[ITERS - 1].append(jnp.sqrt(all_sum(jnp.sum(ortho * ortho)[None])[0]))
    coeffs = least_squares(columns, beta_norm)
    correction = coeffs[0] * krylov[0]
    applied = coeffs[0] * images[0]
    for j in range(1, ITERS):
        correction = correction + coeffs[j] * krylov[j]
        applied = applied + coeffs[j] * images[j]
    residual = rhs_field - applied
    return (correction, residual)


def solution(mesh):
    return jax.shard_map(
        per_device,
        mesh=mesh,
        in_specs=(
            P("harm", "space"),
            P(None, "space"),
            P(None, "space"),
            P(None, None, "space"),
            P("space"),
            P("space"),
        ),
        out_specs=(P("harm", "space"), P("harm", "space")),
        check_vma=False,
    )
```

```python
import jax
import jax.numpy as jnp
from jax import lax
from jax.sharding import PartitionSpec as P

IF = 64
ITERS = 8


def with_halo(array, sides, width):
    for axis, dim in sides:
        count, length = (lax.axis_size(axis), array.shape[dim])
        up = [(i, (i + 1) % count) for i in range(count)]
        down = [(j, i) for i, j in up]
        last = lax.slice_in_dim(array, length - width, length, axis=dim)
        leading = lax.slice_in_dim(array, 0, width, axis=dim)
        before = lax.ppermute(last, axis, up)
        after = lax.ppermute(leading, axis, down)
        array = jnp.concatenate([before, array, after], axis=dim)
    return array


def swap_pairs(vector_in):
    shaped = vector_in.reshape(vector_in.shape[0] // 2, 2, vector_in.shape[1])
    return shaped[:, ::-1, :].reshape(vector_in.shape)


def fourier_tables(harmonics):
    index_vals = jnp.arange(harmonics, dtype=jnp.int32)
    product_mod = jnp.mod(index_vals[:, None] * index_vals[None, :], harmonics).astype(jnp.float32)
    phase = 2.0 * jnp.pi * product_mod / harmonics
    return (jnp.cos(phase), jnp.sin(phase))


def matmul_high(left, right):
    return jnp.dot(left, right, precision=lax.Precision.HIGHEST, preferred_element_type=jnp.float32)


def least_squares(columns, beta_norm):
    steps_total = len(columns)
    rot_cos, rot_sin = ([], [])
    target = [beta_norm] + [jnp.zeros((), jnp.float32)] * steps_total
    triangle = []
    for j in range(steps_total):
        column_vals = list(columns[j])
        for i in range(j):
            first, second = (column_vals[i], column_vals[i + 1])
            column_vals[i] = rot_cos[i] * first + rot_sin[i] * second
            column_vals[i + 1] = rot_cos[i] * second - rot_sin[i] * first
        radius = jnp.sqrt(column_vals[j] * column_vals[j] + column_vals[j + 1] * column_vals[j + 1])
        cosine = column_vals[j] / radius
        sine_val = column_vals[j + 1] / radius
        rot_cos.append(cosine)
        rot_sin.append(sine_val)
        column_vals[j] = radius
        target[j + 1] = -sine_val * target[j]
        target[j] = cosine * target[j]
        triangle.append(column_vals[: j + 1])
    coeffs = [None] * steps_total
    for j in reversed(range(steps_total)):
        running = target[j]
        for k in range(j + 1, steps_total):
            running = running - triangle[k][j] * coeffs[k]
        coeffs[j] = running / triangle[j][j]
    return coeffs


def all_sum(values):
    for axis in ("harm", "space"):
        count = lax.axis_size(axis)
        if count & (count - 1):
            values = lax.psum(values, axis)
            continue
        stride = 1
        while stride < count:
            values = values + lax.ppermute(values, axis, [(i, i ^ stride) for i in range(count)])
            stride *= 2
    return values


def per_device(rhs_field, neighbors, nu_mean, nu_ripple, mass_coeff, eddy_coeff):
    block, nodes_own = rhs_field.shape
    harmonics = nu_ripple.shape[0]
    harm_count = lax.axis_size("harm")
    harm_index = lax.axis_index("harm")
    chunk = nodes_own // harm_count
    devices = harm_count * lax.axis_size("space")
    total_nodes = chunk * devices
    reach = -(-IF // chunk)
    block_index = lax.axis_index("space") * harm_count + harm_index
    take = lambda array: lax.dynamic_slice_in_dim(array, harm_index * chunk, chunk, array.ndim - 1)
    kernel = take(nu_ripple).at[0].add(take(nu_mean))
    mass = take(mass_coeff)
    eddy = take(eddy_coeff)
    cos_table, sin_table = fourier_tables(harmonics)
    relative = jnp.mod(take(neighbors) - block_index * chunk, total_nodes)
    relative = jnp.where(relative >= total_nodes - reach * chunk, relative - total_nodes, relative)
    ext_index = relative + reach * chunk
    all_harm = jnp.arange(harmonics)
    harm_order = (all_harm // 2 + 1).astype(jnp.float32)
    sign_vals = jnp.where(all_harm % 2 == 0, 1.0, -1.0).astype(jnp.float32)
    factor = 4.0 * harm_order / harmonics * sign_vals
    kernel_flat = kernel.reshape(harmonics, -1)
    kernel_real = matmul_high(cos_table, kernel_flat)
    kernel_imag = -matmul_high(sin_table, kernel_flat)

    def device_of(b):
        b = b % devices
        return (b % harm_count) * lax.axis_size("space") + b // harm_count

    def shifted(vector_in, step):
        pairs = [(device_of(b), device_of(b + step)) for b in range(devices)]
        return lax.ppermute(vector_in, ("harm", "space"), pairs)

    def operate(vector_in):
        pieces = [shifted(vector_in, r) for r in range(reach, 0, -1)]
        pieces += [vector_in] + [shifted(vector_in, -r) for r in range(1, reach + 1)]
        extended = jnp.concatenate(pieces, axis=1)
        gradients = vector_in[:, None, :] - extended[:, ext_index]
        grad_flat = gradients.reshape(harmonics, -1)
        spec_real = matmul_high(cos_table, grad_flat)
        spec_imag = -matmul_high(sin_table, grad_flat)
        prod_real = spec_real * kernel_real - spec_imag * kernel_imag
        prod_imag = spec_real * kernel_imag + spec_imag * kernel_real
        fluxes = (matmul_high(cos_table, prod_real) - matmul_high(sin_table, prod_imag)) / harmonics
        fluxes = fluxes.reshape(gradients.shape)
        return (
            jnp.sum(fluxes, axis=1)
            + mass[None, :] * vector_in
            + eddy[None, :] * factor[:, None] * swap_pairs(vector_in)
        )

    rhs_field = lax.all_to_all(rhs_field, "harm", split_axis=1, concat_axis=0, tiled=True)
    local_rows = lambda rows, other: jnp.sum(jnp.stack(rows) * other[None], axis=(1, 2))
    sums = all_sum(jnp.concatenate([local_rows([rhs_field], rhs_field), local_rows([rhs_field], image := operate(rhs_field))]))
    beta_norm = jnp.sqrt(sums[0])
    krylov = [rhs_field / beta_norm]
    images = [image / beta_norm]
    columns = [[sums[1] / beta_norm / beta_norm]]
    ortho = images[0] - columns[0][0] * krylov[0]
    for j in range(1, ITERS):
        image = operate(ortho)
        sums = all_sum(
            jnp.concatenate([local_rows([ortho], ortho), local_rows(krylov + [ortho], image)])
        )
        length = jnp.sqrt(sums[0])
        columns[j - 1].append(length)
        krylov.append(ortho / length)
        images.append(image / length)
        projected = [sums[1 + i] / length for i in range(j)] + [sums[1 + j] / length / length]
        columns.append(projected)
        ortho = images[j]
        for i in range(j + 1):
            ortho = ortho - projected[i] * krylov[i]
    columns[ITERS - 1].append(jnp.sqrt(all_sum(jnp.sum(ortho * ortho)[None])[0]))
    coeffs = least_squares(columns, beta_norm)
    correction = coeffs[0] * krylov[0]
    applied = coeffs[0] * images[0]
    for j in range(1, ITERS):
        correction = correction + coeffs[j] * krylov[j]
        applied = applied + coeffs[j] * images[j]
    residual = rhs_field - applied
    both = lax.all_to_all(jnp.stack([correction, residual]), "harm", split_axis=1, concat_axis=2, tiled=True)
    return (both[0], both[1])


def solution(mesh):
    return jax.shard_map(
        per_device,
        mesh=mesh,
        in_specs=(
            P("harm", "space"),
            P(None, "space"),
            P(None, "space"),
            P(None, None, "space"),
            P("space"),
            P("space"),
        ),
        out_specs=(P("harm", "space"), P("harm", "space")),
        check_vma=False,
    )
```

```python
import jax
import jax.numpy as jnp
from jax import lax
from jax.sharding import PartitionSpec as P

IF = 64
ITERS = 8


def with_halo(array, sides, width):
    for axis, dim in sides:
        count, length = (lax.axis_size(axis), array.shape[dim])
        up = [(i, (i + 1) % count) for i in range(count)]
        down = [(j, i) for i, j in up]
        last = lax.slice_in_dim(array, length - width, length, axis=dim)
        leading = lax.slice_in_dim(array, 0, width, axis=dim)
        before = lax.ppermute(last, axis, up)
        after = lax.ppermute(leading, axis, down)
        array = jnp.concatenate([before, array, after], axis=dim)
    return array


def swap_pairs(vector_in):
    shaped = vector_in.reshape(vector_in.shape[0] // 2, 2, vector_in.shape[1])
    return shaped[:, ::-1, :].reshape(vector_in.shape)


def fourier_tables(harmonics):
    index_vals = jnp.arange(harmonics, dtype=jnp.int32)
    product_mod = jnp.mod(index_vals[:, None] * index_vals[None, :], harmonics).astype(jnp.float32)
    phase = 2.0 * jnp.pi * product_mod / harmonics
    return (jnp.cos(phase), jnp.sin(phase))


def matmul_high(left, right):
    return jnp.dot(left, right, precision=lax.Precision.HIGHEST, preferred_element_type=jnp.float32)


def least_squares(columns, beta_norm):
    steps_total = len(columns)
    rot_cos, rot_sin = ([], [])
    target = [beta_norm] + [jnp.zeros((), jnp.float32)] * steps_total
    triangle = []
    for j in range(steps_total):
        column_vals = list(columns[j])
        for i in range(j):
            first, second = (column_vals[i], column_vals[i + 1])
            column_vals[i] = rot_cos[i] * first + rot_sin[i] * second
            column_vals[i + 1] = rot_cos[i] * second - rot_sin[i] * first
        radius = jnp.sqrt(column_vals[j] * column_vals[j] + column_vals[j + 1] * column_vals[j + 1])
        cosine = column_vals[j] / radius
        sine_val = column_vals[j + 1] / radius
        rot_cos.append(cosine)
        rot_sin.append(sine_val)
        column_vals[j] = radius
        target[j + 1] = -sine_val * target[j]
        target[j] = cosine * target[j]
        triangle.append(column_vals[: j + 1])
    coeffs = [None] * steps_total
    for j in reversed(range(steps_total)):
        running = target[j]
        for k in range(j + 1, steps_total):
            running = running - triangle[k][j] * coeffs[k]
        coeffs[j] = running / triangle[j][j]
    return coeffs


def all_sum(values):
    for axis in ("space",):
        count = lax.axis_size(axis)
        if count & (count - 1):
            values = lax.psum(values, axis)
            continue
        stride = 1
        while stride < count:
            values = values + lax.ppermute(values, axis, [(i, i ^ stride) for i in range(count)])
            stride *= 2
    return values


def per_device(rhs_field, neighbors, nu_mean, nu_ripple, mass_coeff, eddy_coeff):
    block, nodes_own = rhs_field.shape
    harmonics = nu_ripple.shape[0]
    harm_index = lax.axis_index("harm")
    halo_width = IF
    kernel = nu_ripple.at[0].add(nu_mean)
    cos_table, sin_table = fourier_tables(harmonics)
    total_nodes = nodes_own * lax.axis_size("space")
    relative = jnp.mod(neighbors - lax.axis_index("space") * nodes_own, total_nodes)
    relative = jnp.where(relative >= total_nodes - halo_width, relative - total_nodes, relative)
    ext_index = relative + halo_width
    all_harm = jnp.arange(harmonics)
    harm_order = (all_harm // 2 + 1).astype(jnp.float32)
    sign_vals = jnp.where(all_harm % 2 == 0, 1.0, -1.0).astype(jnp.float32)
    factor = 4.0 * harm_order / harmonics * sign_vals
    kernel_flat = kernel.reshape(harmonics, -1)
    kernel_real = matmul_high(cos_table, kernel_flat)
    kernel_imag = -matmul_high(sin_table, kernel_flat)

    def operate(vector_in):
        extended = with_halo(vector_in, (("space", 1),), halo_width)
        gradients = vector_in[:, None, :] - extended[:, ext_index]
        grad_flat = gradients.reshape(harmonics, -1)
        spec_real = matmul_high(cos_table, grad_flat)
        spec_imag = -matmul_high(sin_table, grad_flat)
        prod_real = spec_real * kernel_real - spec_imag * kernel_imag
        prod_imag = spec_real * kernel_imag + spec_imag * kernel_real
        fluxes = (matmul_high(cos_table, prod_real) - matmul_high(sin_table, prod_imag)) / harmonics
        fluxes = fluxes.reshape(gradients.shape)
        return (
            jnp.sum(fluxes, axis=1)
            + mass_coeff[None, :] * vector_in
            + eddy_coeff[None, :] * factor[:, None] * swap_pairs(vector_in)
        )

    rhs_field = lax.all_gather(rhs_field, "harm", axis=0, tiled=True)
    local_rows = lambda rows, other: jnp.sum(jnp.stack(rows) * other[None], axis=(1, 2))
    sums = all_sum(jnp.concatenate([local_rows([rhs_field], rhs_field), local_rows([rhs_field], image := operate(rhs_field))]))
    beta_norm = jnp.sqrt(sums[0])
    krylov = [rhs_field / beta_norm]
    images = [image / beta_norm]
    columns = [[sums[1] / beta_norm / beta_norm]]
    ortho = images[0] - columns[0][0] * krylov[0]
    for j in range(1, ITERS):
        image = operate(ortho)
        sums = all_sum(
            jnp.concatenate([local_rows([ortho], ortho), local_rows(krylov + [ortho], image)])
        )
        length = jnp.sqrt(sums[0])
        columns[j - 1].append(length)
        krylov.append(ortho / length)
        images.append(image / length)
        projected = [sums[1 + i] / length for i in range(j)] + [sums[1 + j] / length / length]
        columns.append(projected)
        ortho = images[j]
        for i in range(j + 1):
            ortho = ortho - projected[i] * krylov[i]
    columns[ITERS - 1].append(jnp.sqrt(all_sum(jnp.sum(ortho * ortho)[None])[0]))
    coeffs = least_squares(columns, beta_norm)
    correction = coeffs[0] * krylov[0]
    applied = coeffs[0] * images[0]
    for j in range(1, ITERS):
        correction = correction + coeffs[j] * krylov[j]
        applied = applied + coeffs[j] * images[j]
    residual = rhs_field - applied
    own = lambda array: lax.dynamic_slice_in_dim(array, harm_index * block, block, 0)
    return (own(correction), own(residual))


def solution(mesh):
    return jax.shard_map(
        per_device,
        mesh=mesh,
        in_specs=(
            P("harm", "space"),
            P(None, "space"),
            P(None, "space"),
            P(None, None, "space"),
            P("space"),
            P("space"),
        ),
        out_specs=(P("harm", "space"), P("harm", "space")),
        check_vma=False,
    )
```

```python
import jax
import jax.numpy as jnp
from jax import lax
from jax.sharding import PartitionSpec as P

IF = 64
ITERS = 8


def with_halo(array, sides, width):
    for axis, dim in sides:
        count, length = (lax.axis_size(axis), array.shape[dim])
        up = [(i, (i + 1) % count) for i in range(count)]
        down = [(j, i) for i, j in up]
        last = lax.slice_in_dim(array, length - width, length, axis=dim)
        leading = lax.slice_in_dim(array, 0, width, axis=dim)
        before = lax.ppermute(last, axis, up)
        after = lax.ppermute(leading, axis, down)
        array = jnp.concatenate([before, array, after], axis=dim)
    return array


def swap_pairs(vector_in):
    shaped = vector_in.reshape(vector_in.shape[0] // 2, 2, vector_in.shape[1])
    return shaped[:, ::-1, :].reshape(vector_in.shape)


def fourier_tables(harmonics):
    index_vals = jnp.arange(harmonics, dtype=jnp.int32)
    product_mod = jnp.mod(index_vals[:, None] * index_vals[None, :], harmonics).astype(jnp.float32)
    phase = 2.0 * jnp.pi * product_mod / harmonics
    return (jnp.cos(phase), jnp.sin(phase))


def matmul_high(left, right):
    return jnp.dot(left, right, precision=lax.Precision.HIGHEST, preferred_element_type=jnp.float32)


def least_squares(columns, beta_norm):
    steps_total = len(columns)
    rot_cos, rot_sin = ([], [])
    target = [beta_norm] + [jnp.zeros((), jnp.float32)] * steps_total
    triangle = []
    for j in range(steps_total):
        column_vals = list(columns[j])
        for i in range(j):
            first, second = (column_vals[i], column_vals[i + 1])
            column_vals[i] = rot_cos[i] * first + rot_sin[i] * second
            column_vals[i + 1] = rot_cos[i] * second - rot_sin[i] * first
        radius = jnp.sqrt(column_vals[j] * column_vals[j] + column_vals[j + 1] * column_vals[j + 1])
        cosine = column_vals[j] / radius
        sine_val = column_vals[j + 1] / radius
        rot_cos.append(cosine)
        rot_sin.append(sine_val)
        column_vals[j] = radius
        target[j + 1] = -sine_val * target[j]
        target[j] = cosine * target[j]
        triangle.append(column_vals[: j + 1])
    coeffs = [None] * steps_total
    for j in reversed(range(steps_total)):
        running = target[j]
        for k in range(j + 1, steps_total):
            running = running - triangle[k][j] * coeffs[k]
        coeffs[j] = running / triangle[j][j]
    return coeffs


def all_sum(values):
    for axis in ("space",):
        count = lax.axis_size(axis)
        if count & (count - 1):
            values = lax.psum(values, axis)
            continue
        stride = 1
        while stride < count:
            values = values + lax.ppermute(values, axis, [(i, i ^ stride) for i in range(count)])
            stride *= 2
    return values


def per_device(rhs_field, neighbors, nu_mean, nu_ripple, mass_coeff, eddy_coeff):
    block, nodes_own = rhs_field.shape
    harmonics = nu_ripple.shape[0]
    harm_index = lax.axis_index("harm")
    halo_width = IF
    kernel = nu_ripple.at[0].add(nu_mean)
    cos_table, sin_table = fourier_tables(harmonics)
    total_nodes = nodes_own * lax.axis_size("space")
    relative = jnp.mod(neighbors - lax.axis_index("space") * nodes_own, total_nodes)
    relative = jnp.where(relative >= total_nodes - halo_width, relative - total_nodes, relative)
    ext_index = relative + halo_width
    all_harm = jnp.arange(harmonics)
    harm_order = (all_harm // 2 + 1).astype(jnp.float32)
    sign_vals = jnp.where(all_harm % 2 == 0, 1.0, -1.0).astype(jnp.float32)
    factor = 4.0 * harm_order / harmonics * sign_vals
    kernel_flat = kernel.reshape(harmonics, -1)
    kernel_real = matmul_high(cos_table, kernel_flat)
    kernel_imag = -matmul_high(sin_table, kernel_flat)

    def extend(vector_in):
        return with_halo(vector_in, (("space", 1),), halo_width)

    def inner(extended):
        return lax.slice_in_dim(extended, halo_width, halo_width + nodes_own, axis=1)

    def operate(extended):
        vector_in = inner(extended)
        gradients = vector_in[:, None, :] - extended[:, ext_index]
        grad_flat = gradients.reshape(harmonics, -1)
        spec_real = matmul_high(cos_table, grad_flat)
        spec_imag = -matmul_high(sin_table, grad_flat)
        prod_real = spec_real * kernel_real - spec_imag * kernel_imag
        prod_imag = spec_real * kernel_imag + spec_imag * kernel_real
        fluxes = (matmul_high(cos_table, prod_real) - matmul_high(sin_table, prod_imag)) / harmonics
        fluxes = fluxes.reshape(gradients.shape)
        return (
            jnp.sum(fluxes, axis=1)
            + mass_coeff[None, :] * vector_in
            + eddy_coeff[None, :] * factor[:, None] * swap_pairs(vector_in)
        )

    rhs_field = lax.all_gather(rhs_field, "harm", axis=0, tiled=True)
    local_rows = lambda rows, other: jnp.sum(jnp.stack(rows) * other[None], axis=(1, 2))
    rhs_ext = extend(rhs_field)
    image = operate(rhs_ext)
    image_ext = extend(image)
    sums = all_sum(jnp.concatenate([local_rows([rhs_field], rhs_field), local_rows([rhs_field], image)]))
    beta_norm = jnp.sqrt(sums[0])
    krylov_ext = [rhs_ext / beta_norm]
    krylov = [inner(krylov_ext[0])]
    images = [image / beta_norm]
    columns = [[sums[1] / beta_norm / beta_norm]]
    ortho_ext = image_ext / beta_norm - columns[0][0] * krylov_ext[0]
    for j in range(1, ITERS):
        ortho = inner(ortho_ext)
        image = operate(ortho_ext)
        last = j + 1 == ITERS
        if not last:
            image_ext = extend(image)
        sums = all_sum(
            jnp.concatenate([local_rows([ortho], ortho), local_rows(krylov + [ortho], image)])
        )
        length = jnp.sqrt(sums[0])
        columns[j - 1].append(length)
        krylov_ext.append(ortho_ext / length)
        krylov.append(inner(krylov_ext[j]))
        images.append(image / length)
        projected = [sums[1 + i] / length for i in range(j)] + [sums[1 + j] / length / length]
        columns.append(projected)
        if last:
            ortho = images[j]
            for i in range(j + 1):
                ortho = ortho - projected[i] * krylov[i]
        else:
            ortho_ext = image_ext / length
            for i in range(j + 1):
                ortho_ext = ortho_ext - projected[i] * krylov_ext[i]
    columns[ITERS - 1].append(jnp.sqrt(all_sum(jnp.sum(ortho * ortho)[None])[0]))
    coeffs = least_squares(columns, beta_norm)
    correction = coeffs[0] * krylov[0]
    applied = coeffs[0] * images[0]
    for j in range(1, ITERS):
        correction = correction + coeffs[j] * krylov[j]
        applied = applied + coeffs[j] * images[j]
    residual = rhs_field - applied
    own = lambda array: lax.dynamic_slice_in_dim(array, harm_index * block, block, 0)
    return (own(correction), own(residual))


def solution(mesh):
    return jax.shard_map(
        per_device,
        mesh=mesh,
        in_specs=(
            P("harm", "space"),
            P(None, "space"),
            P(None, "space"),
            P(None, None, "space"),
            P("space"),
            P("space"),
        ),
        out_specs=(P("harm", "space"), P("harm", "space")),
        check_vma=False,
    )
```

```python
import jax
import jax.numpy as jnp
from jax import lax
from jax.sharding import PartitionSpec as P

IF = 64
ITERS = 8


def with_halo(array, sides, width):
    for axis, dim in sides:
        count, length = (lax.axis_size(axis), array.shape[dim])
        up = [(i, (i + 1) % count) for i in range(count)]
        down = [(j, i) for i, j in up]
        last = lax.slice_in_dim(array, length - width, length, axis=dim)
        leading = lax.slice_in_dim(array, 0, width, axis=dim)
        before = lax.ppermute(last, axis, up)
        after = lax.ppermute(leading, axis, down)
        array = jnp.concatenate([before, array, after], axis=dim)
    return array


def swap_pairs(vector_in):
    shaped = vector_in.reshape(vector_in.shape[0] // 2, 2, vector_in.shape[1])
    return shaped[:, ::-1, :].reshape(vector_in.shape)


def fourier_tables(harmonics):
    index_vals = jnp.arange(harmonics, dtype=jnp.int32)
    product_mod = jnp.mod(index_vals[:, None] * index_vals[None, :], harmonics).astype(jnp.float32)
    phase = 2.0 * jnp.pi * product_mod / harmonics
    return (jnp.cos(phase), jnp.sin(phase))


def matmul_high(left, right):
    return jnp.dot(left, right, precision=lax.Precision.HIGHEST, preferred_element_type=jnp.float32)


def least_squares(columns, beta_norm):
    steps_total = len(columns)
    rot_cos, rot_sin = ([], [])
    target = [beta_norm] + [jnp.zeros((), jnp.float32)] * steps_total
    triangle = []
    for j in range(steps_total):
        column_vals = list(columns[j])
        for i in range(j):
            first, second = (column_vals[i], column_vals[i + 1])
            column_vals[i] = rot_cos[i] * first + rot_sin[i] * second
            column_vals[i + 1] = rot_cos[i] * second - rot_sin[i] * first
        radius = jnp.sqrt(column_vals[j] * column_vals[j] + column_vals[j + 1] * column_vals[j + 1])
        cosine = column_vals[j] / radius
        sine_val = column_vals[j + 1] / radius
        rot_cos.append(cosine)
        rot_sin.append(sine_val)
        column_vals[j] = radius
        target[j + 1] = -sine_val * target[j]
        target[j] = cosine * target[j]
        triangle.append(column_vals[: j + 1])
    coeffs = [None] * steps_total
    for j in reversed(range(steps_total)):
        running = target[j]
        for k in range(j + 1, steps_total):
            running = running - triangle[k][j] * coeffs[k]
        coeffs[j] = running / triangle[j][j]
    return coeffs


def all_sum(values):
    for axis in ("space",):
        count = lax.axis_size(axis)
        if count & (count - 1):
            values = lax.psum(values, axis)
            continue
        stride = 1
        while stride < count:
            values = values + lax.ppermute(values, axis, [(i, i ^ stride) for i in range(count)])
            stride *= 2
    return values


def per_device(rhs_field, neighbors, nu_mean, nu_ripple, mass_coeff, eddy_coeff):
    block, nodes_own = rhs_field.shape
    harmonics = nu_ripple.shape[0]
    harm_index = lax.axis_index("harm")
    halo_width = IF
    kernel = nu_ripple.at[0].add(nu_mean)
    cos_table, sin_table = fourier_tables(harmonics)
    total_nodes = nodes_own * lax.axis_size("space")
    relative = jnp.mod(neighbors - lax.axis_index("space") * nodes_own, total_nodes)
    relative = jnp.where(relative >= total_nodes - halo_width, relative - total_nodes, relative)
    ext_index = relative + halo_width
    select = (ext_index.reshape(1, -1) == jnp.arange(nodes_own + 2 * halo_width)[:, None]).astype(jnp.float32)
    all_harm = jnp.arange(harmonics)
    harm_order = (all_harm // 2 + 1).astype(jnp.float32)
    sign_vals = jnp.where(all_harm % 2 == 0, 1.0, -1.0).astype(jnp.float32)
    factor = 4.0 * harm_order / harmonics * sign_vals
    kernel_flat = kernel.reshape(harmonics, -1)
    kernel_real = matmul_high(cos_table, kernel_flat)
    kernel_imag = -matmul_high(sin_table, kernel_flat)

    def extend(vector_in):
        return with_halo(vector_in, (("space", 1),), halo_width)

    def inner(extended):
        return lax.slice_in_dim(extended, halo_width, halo_width + nodes_own, axis=1)

    def operate(extended):
        vector_in = inner(extended)
        gathered = matmul_high(extended, select).reshape(harmonics, -1, nodes_own)
        gradients = vector_in[:, None, :] - gathered
        grad_flat = gradients.reshape(harmonics, -1)
        spec_real = matmul_high(cos_table, grad_flat)
        spec_imag = -matmul_high(sin_table, grad_flat)
        prod_real = spec_real * kernel_real - spec_imag * kernel_imag
        prod_imag = spec_real * kernel_imag + spec_imag * kernel_real
        fluxes = (matmul_high(cos_table, prod_real) - matmul_high(sin_table, prod_imag)) / harmonics
        fluxes = fluxes.reshape(gradients.shape)
        return (
            jnp.sum(fluxes, axis=1)
            + mass_coeff[None, :] * vector_in
            + eddy_coeff[None, :] * factor[:, None] * swap_pairs(vector_in)
        )

    rhs_field = lax.all_gather(rhs_field, "harm", axis=0, tiled=True)
    local_rows = lambda rows, other: jnp.sum(jnp.stack(rows) * other[None], axis=(1, 2))
    rhs_ext = extend(rhs_field)
    image = operate(rhs_ext)
    image_ext = extend(image)
    sums = all_sum(jnp.concatenate([local_rows([rhs_field], rhs_field), local_rows([rhs_field], image)]))
    beta_norm = jnp.sqrt(sums[0])
    krylov_ext = [rhs_ext / beta_norm]
    krylov = [inner(krylov_ext[0])]
    images = [image / beta_norm]
    columns = [[sums[1] / beta_norm / beta_norm]]
    ortho_ext = image_ext / beta_norm - columns[0][0] * krylov_ext[0]
    for j in range(1, ITERS):
        ortho = inner(ortho_ext)
        image = operate(ortho_ext)
        last = j + 1 == ITERS
        if not last:
            image_ext = extend(image)
        sums = all_sum(
            jnp.concatenate([local_rows([ortho], ortho), local_rows(krylov + [ortho], image)])
        )
        length = jnp.sqrt(sums[0])
        columns[j - 1].append(length)
        krylov_ext.append(ortho_ext / length)
        krylov.append(inner(krylov_ext[j]))
        images.append(image / length)
        projected = [sums[1 + i] / length for i in range(j)] + [sums[1 + j] / length / length]
        columns.append(projected)
        if last:
            ortho = images[j]
            for i in range(j + 1):
                ortho = ortho - projected[i] * krylov[i]
        else:
            ortho_ext = image_ext / length
            for i in range(j + 1):
                ortho_ext = ortho_ext - projected[i] * krylov_ext[i]
    columns[ITERS - 1].append(jnp.sqrt(all_sum(jnp.sum(ortho * ortho)[None])[0]))
    coeffs = least_squares(columns, beta_norm)
    correction = coeffs[0] * krylov[0]
    applied = coeffs[0] * images[0]
    for j in range(1, ITERS):
        correction = correction + coeffs[j] * krylov[j]
        applied = applied + coeffs[j] * images[j]
    residual = rhs_field - applied
    own = lambda array: lax.dynamic_slice_in_dim(array, harm_index * block, block, 0)
    return (own(correction), own(residual))


def solution(mesh):
    return jax.shard_map(
        per_device,
        mesh=mesh,
        in_specs=(
            P("harm", "space"),
            P(None, "space"),
            P(None, "space"),
            P(None, None, "space"),
            P("space"),
            P("space"),
        ),
        out_specs=(P("harm", "space"), P("harm", "space")),
        check_vma=False,
    )
```

```python
import jax
import jax.numpy as jnp
from jax import lax
from jax.sharding import PartitionSpec as P

IF = 64
ITERS = 8


def with_halo(array, sides, width):
    for axis, dim in sides:
        count, length = (lax.axis_size(axis), array.shape[dim])
        up = [(i, (i + 1) % count) for i in range(count)]
        down = [(j, i) for i, j in up]
        last = lax.slice_in_dim(array, length - width, length, axis=dim)
        leading = lax.slice_in_dim(array, 0, width, axis=dim)
        before = lax.ppermute(last, axis, up)
        after = lax.ppermute(leading, axis, down)
        array = jnp.concatenate([before, array, after], axis=dim)
    return array


def swap_pairs(vector_in):
    shaped = vector_in.reshape(vector_in.shape[0] // 2, 2, vector_in.shape[1])
    return shaped[:, ::-1, :].reshape(vector_in.shape)


def fourier_tables(harmonics):
    index_vals = jnp.arange(harmonics, dtype=jnp.int32)
    product_mod = jnp.mod(index_vals[:, None] * index_vals[None, :], harmonics).astype(jnp.float32)
    phase = 2.0 * jnp.pi * product_mod / harmonics
    return (jnp.cos(phase), jnp.sin(phase))


def matmul_high(left, right):
    return jnp.dot(left, right, precision=lax.Precision.HIGHEST, preferred_element_type=jnp.float32)


def least_squares(columns, beta_norm):
    steps_total = len(columns)
    rot_cos, rot_sin = ([], [])
    target = [beta_norm] + [jnp.zeros((), jnp.float32)] * steps_total
    triangle = []
    for j in range(steps_total):
        column_vals = list(columns[j])
        for i in range(j):
            first, second = (column_vals[i], column_vals[i + 1])
            column_vals[i] = rot_cos[i] * first + rot_sin[i] * second
            column_vals[i + 1] = rot_cos[i] * second - rot_sin[i] * first
        radius = jnp.sqrt(column_vals[j] * column_vals[j] + column_vals[j + 1] * column_vals[j + 1])
        cosine = column_vals[j] / radius
        sine_val = column_vals[j + 1] / radius
        rot_cos.append(cosine)
        rot_sin.append(sine_val)
        column_vals[j] = radius
        target[j + 1] = -sine_val * target[j]
        target[j] = cosine * target[j]
        triangle.append(column_vals[: j + 1])
    coeffs = [None] * steps_total
    for j in reversed(range(steps_total)):
        running = target[j]
        for k in range(j + 1, steps_total):
            running = running - triangle[k][j] * coeffs[k]
        coeffs[j] = running / triangle[j][j]
    return coeffs


def all_sum(values):
    for axis in ("space",):
        count = lax.axis_size(axis)
        if count & (count - 1):
            values = lax.psum(values, axis)
            continue
        stride = 1
        while stride < count:
            values = values + lax.ppermute(values, axis, [(i, i ^ stride) for i in range(count)])
            stride *= 2
    return values


def gather_harmonics(values, position):
    count = lax.axis_size("harm")
    stride = 1
    while stride < count:
        other = lax.ppermute(values, "harm", [(i, i ^ stride) for i in range(count)])
        low = (position // stride) % 2 == 0
        values = jnp.where(low, jnp.concatenate([values, other]), jnp.concatenate([other, values]))
        stride *= 2
    return values


def per_device(rhs_field, neighbors, nu_mean, nu_ripple, mass_coeff, eddy_coeff):
    block, nodes_own = rhs_field.shape
    harmonics = nu_ripple.shape[0]
    harm_index = lax.axis_index("harm")
    halo_width = IF
    kernel = nu_ripple.at[0].add(nu_mean)
    cos_table, sin_table = fourier_tables(harmonics)
    total_nodes = nodes_own * lax.axis_size("space")
    relative = jnp.mod(neighbors - lax.axis_index("space") * nodes_own, total_nodes)
    relative = jnp.where(relative >= total_nodes - halo_width, relative - total_nodes, relative)
    ext_index = relative + halo_width
    select = (ext_index.reshape(1, -1) == jnp.arange(nodes_own + 2 * halo_width)[:, None]).astype(jnp.float32)
    all_harm = jnp.arange(harmonics)
    harm_order = (all_harm // 2 + 1).astype(jnp.float32)
    sign_vals = jnp.where(all_harm % 2 == 0, 1.0, -1.0).astype(jnp.float32)
    factor = 4.0 * harm_order / harmonics * sign_vals
    kernel_flat = kernel.reshape(harmonics, -1)
    kernel_real = matmul_high(cos_table, kernel_flat)
    kernel_imag = -matmul_high(sin_table, kernel_flat)

    def extend(vector_in):
        return with_halo(vector_in, (("space", 1),), halo_width)

    def inner(extended):
        return lax.slice_in_dim(extended, halo_width, halo_width + nodes_own, axis=1)

    def operate(extended):
        vector_in = inner(extended)
        gathered = matmul_high(extended, select).reshape(harmonics, -1, nodes_own)
        gradients = vector_in[:, None, :] - gathered
        grad_flat = gradients.reshape(harmonics, -1)
        spec_real = matmul_high(cos_table, grad_flat)
        spec_imag = -matmul_high(sin_table, grad_flat)
        prod_real = spec_real * kernel_real - spec_imag * kernel_imag
        prod_imag = spec_real * kernel_imag + spec_imag * kernel_real
        fluxes = (matmul_high(cos_table, prod_real) - matmul_high(sin_table, prod_imag)) / harmonics
        fluxes = fluxes.reshape(gradients.shape)
        return (
            jnp.sum(fluxes, axis=1)
            + mass_coeff[None, :] * vector_in
            + eddy_coeff[None, :] * factor[:, None] * swap_pairs(vector_in)
        )

    rhs_field = gather_harmonics(rhs_field, harm_index)
    local_rows = lambda rows, other: jnp.sum(jnp.stack(rows) * other[None], axis=(1, 2))
    rhs_ext = extend(rhs_field)
    image = operate(rhs_ext)
    image_ext = extend(image)
    sums = all_sum(jnp.concatenate([local_rows([rhs_field], rhs_field), local_rows([rhs_field], image)]))
    beta_norm = jnp.sqrt(sums[0])
    krylov_ext = [rhs_ext / beta_norm]
    krylov = [inner(krylov_ext[0])]
    images = [image / beta_norm]
    columns = [[sums[1] / beta_norm / beta_norm]]
    ortho_ext = image_ext / beta_norm - columns[0][0] * krylov_ext[0]
    for j in range(1, ITERS):
        ortho = inner(ortho_ext)
        image = operate(ortho_ext)
        last = j + 1 == ITERS
        if not last:
            image_ext = extend(image)
        sums = all_sum(
            jnp.concatenate([local_rows([ortho], ortho), local_rows(krylov + [ortho], image)])
        )
        length = jnp.sqrt(sums[0])
        columns[j - 1].append(length)
        krylov_ext.append(ortho_ext / length)
        krylov.append(inner(krylov_ext[j]))
        images.append(image / length)
        projected = [sums[1 + i] / length for i in range(j)] + [sums[1 + j] / length / length]
        columns.append(projected)
        if last:
            ortho = images[j]
            for i in range(j + 1):
                ortho = ortho - projected[i] * krylov[i]
        else:
            ortho_ext = image_ext / length
            for i in range(j + 1):
                ortho_ext = ortho_ext - projected[i] * krylov_ext[i]
    columns[ITERS - 1].append(jnp.sqrt(all_sum(jnp.sum(ortho * ortho)[None])[0]))
    coeffs = least_squares(columns, beta_norm)
    correction = coeffs[0] * krylov[0]
    applied = coeffs[0] * images[0]
    for j in range(1, ITERS):
        correction = correction + coeffs[j] * krylov[j]
        applied = applied + coeffs[j] * images[j]
    residual = rhs_field - applied
    own = lambda array: lax.dynamic_slice_in_dim(array, harm_index * block, block, 0)
    return (own(correction), own(residual))


def solution(mesh):
    return jax.shard_map(
        per_device,
        mesh=mesh,
        in_specs=(
            P("harm", "space"),
            P(None, "space"),
            P(None, "space"),
            P(None, None, "space"),
            P("space"),
            P("space"),
        ),
        out_specs=(P("harm", "space"), P("harm", "space")),
        check_vma=False,
    )
```

```python
import jax
import jax.numpy as jnp
from jax import lax
from jax.sharding import PartitionSpec as P

IF = 64
ITERS = 8


def with_halo(array, sides, width):
    for axis, dim in sides:
        count, length = (lax.axis_size(axis), array.shape[dim])
        up = [(i, (i + 1) % count) for i in range(count)]
        down = [(j, i) for i, j in up]
        last = lax.slice_in_dim(array, length - width, length, axis=dim)
        leading = lax.slice_in_dim(array, 0, width, axis=dim)
        before = lax.ppermute(last, axis, up)
        after = lax.ppermute(leading, axis, down)
        array = jnp.concatenate([before, array, after], axis=dim)
    return array


def swap_pairs(vector_in):
    shaped = vector_in.reshape(vector_in.shape[0] // 2, 2, vector_in.shape[1])
    return shaped[:, ::-1, :].reshape(vector_in.shape)


def fourier_tables(harmonics):
    index_vals = jnp.arange(harmonics, dtype=jnp.int32)
    product_mod = jnp.mod(index_vals[:, None] * index_vals[None, :], harmonics).astype(jnp.float32)
    phase = 2.0 * jnp.pi * product_mod / harmonics
    return (jnp.cos(phase), jnp.sin(phase))


def matmul_high(left, right):
    return jnp.dot(left, right, precision=lax.Precision.HIGHEST, preferred_element_type=jnp.float32)


def least_squares(columns, beta_norm):
    steps_total = len(columns)
    rot_cos, rot_sin = ([], [])
    target = [beta_norm] + [jnp.zeros((), jnp.float32)] * steps_total
    triangle = []
    for j in range(steps_total):
        column_vals = list(columns[j])
        for i in range(j):
            first, second = (column_vals[i], column_vals[i + 1])
            column_vals[i] = rot_cos[i] * first + rot_sin[i] * second
            column_vals[i + 1] = rot_cos[i] * second - rot_sin[i] * first
        radius = jnp.sqrt(column_vals[j] * column_vals[j] + column_vals[j + 1] * column_vals[j + 1])
        cosine = column_vals[j] / radius
        sine_val = column_vals[j + 1] / radius
        rot_cos.append(cosine)
        rot_sin.append(sine_val)
        column_vals[j] = radius
        target[j + 1] = -sine_val * target[j]
        target[j] = cosine * target[j]
        triangle.append(column_vals[: j + 1])
    coeffs = [None] * steps_total
    for j in reversed(range(steps_total)):
        running = target[j]
        for k in range(j + 1, steps_total):
            running = running - triangle[k][j] * coeffs[k]
        coeffs[j] = running / triangle[j][j]
    return coeffs


def all_sum(values):
    for axis in ("space",):
        count = lax.axis_size(axis)
        if count & (count - 1):
            values = lax.psum(values, axis)
            continue
        stride = count // 2
        while stride >= 1:
            values = values + lax.ppermute(values, axis, [(i, i ^ stride) for i in range(count)])
            stride //= 2
    return values


def gather_harmonics(values, position):
    count = lax.axis_size("harm")
    stride = 1
    while stride < count:
        other = lax.ppermute(values, "harm", [(i, i ^ stride) for i in range(count)])
        low = (position // stride) % 2 == 0
        values = jnp.where(low, jnp.concatenate([values, other]), jnp.concatenate([other, values]))
        stride *= 2
    return values


def per_device(rhs_field, neighbors, nu_mean, nu_ripple, mass_coeff, eddy_coeff):
    block, nodes_own = rhs_field.shape
    harmonics = nu_ripple.shape[0]
    harm_index = lax.axis_index("harm")
    halo_width = IF
    kernel = nu_ripple.at[0].add(nu_mean)
    cos_table, sin_table = fourier_tables(harmonics)
    total_nodes = nodes_own * lax.axis_size("space")
    relative = jnp.mod(neighbors - lax.axis_index("space") * nodes_own, total_nodes)
    relative = jnp.where(relative >= total_nodes - halo_width, relative - total_nodes, relative)
    ext_index = relative + halo_width
    select = (ext_index.reshape(1, -1) == jnp.arange(nodes_own + 2 * halo_width)[:, None]).astype(jnp.float32)
    all_harm = jnp.arange(harmonics)
    harm_order = (all_harm // 2 + 1).astype(jnp.float32)
    sign_vals = jnp.where(all_harm % 2 == 0, 1.0, -1.0).astype(jnp.float32)
    factor = 4.0 * harm_order / harmonics * sign_vals
    kernel_flat = kernel.reshape(harmonics, -1)
    kernel_real = matmul_high(cos_table, kernel_flat)
    kernel_imag = -matmul_high(sin_table, kernel_flat)

    def extend(vector_in):
        return with_halo(vector_in, (("space", 1),), halo_width)

    def inner(extended):
        return lax.slice_in_dim(extended, halo_width, halo_width + nodes_own, axis=1)

    def operate(extended):
        vector_in = inner(extended)
        gathered = matmul_high(extended, select).reshape(harmonics, -1, nodes_own)
        gradients = vector_in[:, None, :] - gathered
        grad_flat = gradients.reshape(harmonics, -1)
        spec_real = matmul_high(cos_table, grad_flat)
        spec_imag = -matmul_high(sin_table, grad_flat)
        prod_real = spec_real * kernel_real - spec_imag * kernel_imag
        prod_imag = spec_real * kernel_imag + spec_imag * kernel_real
        fluxes = (matmul_high(cos_table, prod_real) - matmul_high(sin_table, prod_imag)) / harmonics
        fluxes = fluxes.reshape(gradients.shape)
        return (
            jnp.sum(fluxes, axis=1)
            + mass_coeff[None, :] * vector_in
            + eddy_coeff[None, :] * factor[:, None] * swap_pairs(vector_in)
        )

    rhs_field = gather_harmonics(rhs_field, harm_index)
    local_rows = lambda rows, other: jnp.sum(jnp.stack(rows) * other[None], axis=(1, 2))
    rhs_ext = extend(rhs_field)
    image = operate(rhs_ext)
    image_ext = extend(image)
    sums = all_sum(jnp.concatenate([local_rows([rhs_field], rhs_field), local_rows([rhs_field], image)]))
    beta_norm = jnp.sqrt(sums[0])
    krylov_ext = [rhs_ext / beta_norm]
    krylov = [inner(krylov_ext[0])]
    images = [image / beta_norm]
    columns = [[sums[1] / beta_norm / beta_norm]]
    ortho_ext = image_ext / beta_norm - columns[0][0] * krylov_ext[0]
    for j in range(1, ITERS):
      ortho = inner(ortho_ext)
      image = operate(ortho_ext)
      last = j + 1 == ITERS
      if not last:
          image_ext = extend(image)
      sums = all_sum(
          jnp.concatenate([local_rows([ortho], ortho), local_rows(krylov + [ortho], image)])
      )
      length = jnp.sqrt(sums[0])
      columns[j - 1].append(length)
      krylov_ext.append(ortho_ext / length)
      krylov.append(inner(krylov_ext[j]))
      images.append(image / length)
      projected = [sums[1 + i] / length for i in range(j)] + [sums[1 + j] / length / length]
      columns.append(projected)
      if last:
          ortho = images[j]
          for i in range(j + 1):
              ortho = ortho - projected[i] * krylov[i]
      else:
          ortho_ext = image_ext / length
          for i in range(j + 1):
              ortho_ext = ortho_ext - projected[i] * krylov_ext[i]
    columns[ITERS - 1].append(jnp.sqrt(all_sum(jnp.sum(ortho * ortho)[None])[0]))
    coeffs = least_squares(columns, beta_norm)
    correction = coeffs[0] * krylov[0]
    applied = coeffs[0] * images[0]
    for j in range(1, ITERS):
        correction = correction + coeffs[j] * krylov[j]
        applied = applied + coeffs[j] * images[j]
    residual = rhs_field - applied
    own = lambda array: lax.dynamic_slice_in_dim(array, harm_index * block, block, 0)
    return (own(correction), own(residual))


def solution(mesh):
    return jax.shard_map(
        per_device,
        mesh=mesh,
        in_specs=(
            P("harm", "space"),
            P(None, "space"),
            P(None, "space"),
            P(None, None, "space"),
            P("space"),
            P("space"),
        ),
        out_specs=(P("harm", "space"), P("harm", "space")),
        check_vma=False,
    )
```
